128 devices in a mesh: batch: 4 (over y), region: 32 (over x, z, core).
Axes of the slice: x: 4, y: 4, z: 4, core: 2. Of those that a mesh axis runs over, the one named last changes fastest.
Arguments:
- leaves: float32 [256, 4096, 256], P('region', 'batch'), may hold values from -66 to 66
- leaf_order: int32 [32, 8], replicated, may hold values from 0 to 7, each once within a row
- node_order: int32 [32, 4], replicated, may hold values from 0 to 3, each once within a row
- weight_one: float32 [128, 256, 256], P('region'), may hold values from 0.001 to 0.04
- weight_two: float32 [64, 256, 256], P('region'), may hold values from 0.001 to 0.04
- top_adjoint: float32 [64, 4096, 256], P('region', 'batch'), may hold values from -6 to 6
Outputs:
- top_log: float32 [64, 4096, 256], P('region', 'batch')
- leaf_adjoint: float32 [256, 4096, 256], P('region', 'batch')
- grad_one: float32 [128, 256, 256], P('region')
- grad_two: float32 [64, 256, 256], P('region')
The draws below stay inside these ranges and needn't reach their ends.
Inputs may be any that keep to these rules, and one draw needn't show every extreme that they name: Each row of leaf_order is a permutation of 0 to 7. Each row of node_order is a permutation of 0 to 3.
All inputs are finite; a program needn't handle non-finite values.
Results may differ from the reference program's by a relative error of at most 0.0003.
Values sent between devices are 32-bit elements; how exact they have to be, the bound alone decides.
No kernel may reach another device: no remote copies, remote signals or barrier semaphores. Data moves between devices by JAX's collectives and lax.ppermute only.
A program may use at most 128 MiB of HBM per device.

```python
import math
import jax
import jax.numpy as jnp
from jax import lax

K = 256
L_DEV = 8
NODE1_DEV = 4
RDEV = 32
BATCH = 4096
LEAVES = 256
NODES1 = 128
NODES2 = 64


def draw_leaves(key, part):
    base_key, scale_key = jax.random.split(key, 2)
    spread = jnp.exp(jax.random.uniform(scale_key, (LEAVES, 1, K), jnp.float32, -1.15, 1.15))
    base = jnp.clip(jax.random.normal(base_key, (LEAVES, BATCH, K), jnp.float32), -4.0, 4.0)
    return base * spread


def shard_levels(rng, extent, cuts, smallest, top_value):
    level = 1.0
    for dim, blocks in cuts:
        heights = jax.random.uniform(jax.random.fold_in(jax.random.fold_in(rng, 6), dim), (blocks,), jnp.float32, smallest / len(cuts), top_value / len(cuts))
        level = level * jnp.repeat(jnp.exp(heights), extent[dim] // blocks).reshape((-1,) + (1,) * (len(extent) - 1 - dim))
    return level


def gaussian(key, extent, deviation, most, shards=(), held_as=jnp.bfloat16):
    gain = shard_levels(key, extent, shards, -0.22, 0.18) if shards else 1.0
    array = jax.random.normal(key, extent, jnp.float32) * deviation * gain
    return jnp.minimum(jnp.maximum(array, -most), most).astype(held_as)


def setup_inputs(seed: int = 0) -> dict:
    key_of = jax.random.split(jax.random.key(seed), 7)
    return {
        "leaves": draw_leaves(jax.random.fold_in(key_of[6], 71), 0),
        "leaf_order": jax.vmap(lambda own: jax.random.permutation(own, L_DEV))(jax.random.split(key_of[1], RDEV)).reshape((RDEV, L_DEV)).astype(jnp.int32),
        "node_order": jax.vmap(lambda own: jax.random.permutation(own, NODE1_DEV))(jax.random.split(key_of[2], RDEV)).reshape((RDEV, NODE1_DEV)).astype(jnp.int32),
        "weight_one": jnp.clip(jnp.exp(math.log(0.04) - 3.6888794 * jax.random.uniform(key_of[3], (NODES1, K, K), jnp.float32) ** shard_levels(key_of[3], (NODES1, K, K), ((0, 32),), -0.2, 0.2)), 0.001, 0.04),
        "weight_two": jnp.clip(jnp.exp(math.log(0.04) - 3.6888794 * jax.random.uniform(key_of[4], (NODES2, K, K), jnp.float32) ** shard_levels(key_of[4], (NODES2, K, K), ((0, 32),), -0.2, 0.2)), 0.001, 0.04),
        "top_adjoint": gaussian(key_of[5], (NODES2, BATCH, K), 1.0, 6.0, ((0, 32), (1, 4)), jnp.float32),
    }


def node_mix(operands):
    left, right, weight = operands
    summed = left + right
    peak = lax.optimization_barrier(jnp.max(summed, axis=1, keepdims=True))
    scaled = jnp.exp(summed - peak)
    totals = jnp.dot(scaled, weight.T, precision=lax.Precision.HIGHEST, preferred_element_type=jnp.float32)
    return peak + jnp.log(totals)

def level_mix(tiles, order, partner_bit, split, weights):
    devices = order.shape[0]
    slots = order.shape[1]
    rows = tiles.reshape(devices, slots, tiles.shape[1], tiles.shape[2])
    index = jnp.arange(devices, dtype=jnp.int32)
    other = jnp.bitwise_xor(index, jnp.int32(partner_bit))
    left = rows[index[:, None], order[:, :split]]
    right = rows[other[:, None], order[other][:, split:]]
    left = left.reshape(devices * split, tiles.shape[1], tiles.shape[2])
    right = right.reshape(devices * split, tiles.shape[1], tiles.shape[2])
    return lax.map(node_mix, (left, right, weights))

def reference(leaves, leaf_order, node_order, weight_one, weight_two, top_adjoint):

    def forward(leaf_vals, first_w, second_w):
        level_one = level_mix(leaf_vals, leaf_order, 1, L_DEV // 2, first_w)
        return level_mix(level_one, node_order, 2, L_DEV // 4, second_w)
    top_log, pullback = jax.vjp(forward, leaves, weight_one, weight_two)
    leaf_adjoint, grad_one, grad_two = pullback(top_adjoint)
    return (top_log, leaf_adjoint, grad_one, grad_two)
```

```python
import functools

import jax
import jax.numpy as jnp
from jax import lax
from jax.experimental import pallas as pl
from jax.experimental.pallas import tpu as pltpu
from jax.sharding import PartitionSpec as P


HIGHEST = lax.Precision.HIGHEST
VMEM_LIMIT = 48 * 1024 * 1024


def from_partner(value, axis, distance):
    mask = 2**distance
    pairs = [(source, source ^ mask) for source in range(lax.axis_size(axis))]
    return lax.ppermute(value, axis, pairs)


def block(shape, select):
    kind, k = select
    if kind == "table":
        return pl.BlockSpec((None,) + shape, lambda i, t: (t[k], 0, 0))
    return pl.BlockSpec((None,) + shape, lambda i, t: (k, 0, 0))


def whole(shape):
    return pl.BlockSpec(shape, lambda i, t: (0, 0))


ANY = pl.BlockSpec(memory_space=pl.ANY)


def slab_spec(rows, k):
    return pl.BlockSpec((1, rows, k), lambda i, t: (0, 0, 0))


def call(kernel, table, operands, in_specs, out_specs, out_shape, cost, aliases=None, scratch=(), grid=(1,)):
    return pl.pallas_call(
        kernel,
        grid_spec=pltpu.PrefetchScalarGridSpec(
            num_scalar_prefetch=1, grid=grid, in_specs=in_specs, out_specs=out_specs,
            scratch_shapes=list(scratch),
        ),
        out_shape=out_shape,
        input_output_aliases=aliases or {},
        compiler_params=pltpu.CompilerParams(vmem_limit_bytes=VMEM_LIMIT),
        cost_estimate=cost,
    )(table, *operands)


def mix_kernel(table, left, right, weight, out, scaled, totals):
    summed = left[...] + right[...]
    peak = jnp.max(summed, axis=1, keepdims=True)
    p = jnp.exp(summed - peak)
    q = lax.dot_general(p, weight[...], (((1,), (1,)), ((), ())), precision=HIGHEST,
                        preferred_element_type=jnp.float32)
    out[...] = peak + jnp.log(q)
    scaled[...] = p
    totals[...] = q


def mix(table, left, left_sel, right, right_sel, weight, weight_sel):
    rows, k = left.shape[1:]
    o = jax.ShapeDtypeStruct((rows, k), jnp.float32)
    cost = pl.CostEstimate(flops=2 * rows * k * k, transcendentals=2 * rows * k,
                           bytes_accessed=4 * (5 * rows * k + k * k))
    return call(mix_kernel, table, (left, right, weight),
                [block((rows, k), left_sel), block((rows, k), right_sel), block((k, k), weight_sel)],
                [whole((rows, k))] * 3, [o, o, o], cost)


def descend_kernel(placing, own_at, table, adjoint, scaled, totals, weight, *rest):
    if placing == 0:
        counts, spread = rest
    elif placing == 1:
        counts, spread, buffer, sems = rest
    else:
        _, counts, spread, buffer, sems = rest
    ratio = adjoint[...] / totals[...]
    p = scaled[...]
    counts[...] = lax.dot_general(ratio, p, (((0,), (0,)), ((), ())), precision=HIGHEST,
                                  preferred_element_type=jnp.float32)
    spread[...] = p * jnp.dot(ratio, weight[...], precision=HIGHEST, preferred_element_type=jnp.float32)
    if placing == 0:
        return
    c = pltpu.make_async_copy(spread, buffer.at[table[own_at]], sems.at[0])
    c.start()
    c.wait()


def descend(table, adjoint, adjoint_sel, scaled, totals, weight, weight_sel,
            buffer_shape=None, own_at=None, buffer=None):
    rows, k = scaled.shape
    cost = pl.CostEstimate(flops=4 * rows * k * k, transcendentals=0,
                           bytes_accessed=4 * (5 * rows * k + 2 * k * k))
    operands = [adjoint, scaled[None], totals[None], weight]
    in_specs = [block((rows, k), adjoint_sel), block((rows, k), ("fixed", 0)),
                block((rows, k), ("fixed", 0)), block((k, k), weight_sel)]
    out_specs = [whole((k, k)), whole((rows, k))]
    out_shape = [jax.ShapeDtypeStruct((k, k), jnp.float32), jax.ShapeDtypeStruct((rows, k), jnp.float32)]
    placing, aliases, scratch = 0, None, ()
    if buffer_shape is not None:
        placing = 1 if buffer is None else 2
        out_specs.append(ANY)
        out_shape.append(jax.ShapeDtypeStruct(buffer_shape, jnp.float32))
        scratch = (pltpu.SemaphoreType.DMA((1,)),)
        if buffer is not None:
            operands.append(buffer)
            in_specs.append(ANY)
            aliases = {len(operands): 2}
    kernel = functools.partial(descend_kernel, placing, own_at)
    return call(kernel, table, operands, in_specs, out_specs, out_shape, cost, aliases, scratch)


def place_kernel(positions, table, *rest):
    sources, buffer, sems = rest[:len(positions)], rest[len(positions) + 1], rest[-1]
    copies = [pltpu.make_async_copy(src, buffer.at[pl.ds(table[at], 1)], sems.at[n])
              for n, (src, at) in enumerate(zip(sources, positions))]
    for c in copies:
        c.start()
    for c in copies:
        c.wait()


def place(table, buffer, slabs, positions):
    rows, k = slabs[0].shape
    n = len(slabs)
    cost = pl.CostEstimate(flops=0, transcendentals=0, bytes_accessed=8 * rows * k * n)
    return call(functools.partial(place_kernel, tuple(positions)), table,
                tuple(slab[None] for slab in slabs) + (buffer,),
                [slab_spec(rows, k)] * n + [ANY], ANY,
                jax.ShapeDtypeStruct(buffer.shape, buffer.dtype), cost, aliases={n + 1: 0},
                scratch=(pltpu.SemaphoreType.DMA((n,)),))


def grads_kernel(table, late, early, out, sems):
    pairs = [(late, j, j) for j in range(late.shape[0])]
    pairs += [(early, j, late.shape[0] + j) for j in range(early.shape[0])]
    copies = [pltpu.make_async_copy(src.at[pl.ds(j, 1)], out.at[pl.ds(table[at], 1)], sems.at[n])
              for n, (src, j, at) in enumerate(pairs)]
    for c in copies:
        c.start()
    for c in copies:
        c.wait()


def place_grads(table, late, early):
    n, k, _ = late.shape
    m = early.shape[0]
    cost = pl.CostEstimate(flops=0, transcendentals=0, bytes_accessed=8 * (n + m) * k * k)
    spec = lambda a: pl.BlockSpec(a.shape, lambda i, t: (0, 0, 0))
    return call(grads_kernel, table, (late, early), [spec(late), spec(early)], ANY,
                jax.ShapeDtypeStruct((n + m, k, k), jnp.float32), cost,
                scratch=(pltpu.SemaphoreType.DMA((n + m,)),))


def copy_kernel(table, source, out):
    out[...] = source[...]


def select(table, array, at, pieces=1):
    rows, k = array.shape[1:]
    part = rows // pieces
    cost = pl.CostEstimate(flops=0, transcendentals=0, bytes_accessed=8 * rows * k)
    return call(copy_kernel, table, (array,),
                [pl.BlockSpec((None, part, k), lambda i, t: (t[at], i, 0))],
                pl.BlockSpec((part, k), lambda i, t: (i, 0)),
                jax.ShapeDtypeStruct((rows, k), jnp.float32), cost, grid=(pieces,))


def batch_sum(x, axis):
    if lax.axis_size(axis) != 4:
        return lax.psum(x, axis)
    me = lax.axis_index(axis)
    low = jnp.bitwise_and(me, 1) == 0
    high = jnp.bitwise_and(me, 2) == 0
    flat = x.reshape(-1, x.shape[-1])
    half = flat.shape[0] // 2
    a, b = flat[:half], flat[half:]
    got = from_partner(jnp.where(low, b, a), axis, 0)
    keep = jnp.where(low, a, b) + got
    quarter = half // 2
    c, d = keep[:quarter], keep[quarter:]
    got = from_partner(jnp.where(high, d, c), axis, 1)
    mine = jnp.where(high, c, d) + got
    theirs = from_partner(mine, axis, 1)
    keep = jnp.where(high, jnp.concatenate([mine, theirs]), jnp.concatenate([theirs, mine]))
    theirs = from_partner(keep, axis, 0)
    flat = jnp.where(low, jnp.concatenate([keep, theirs]), jnp.concatenate([theirs, keep]))
    return flat.reshape(x.shape)


def local(leaves, leaf_order, node_order, weight_one, weight_two, top_adjoint):
    here = lax.axis_index("region")
    across = jnp.bitwise_xor(here, jnp.int32(1))
    first = weight_one.shape[0]
    second = weight_two.shape[0]
    own_leaf = lax.dynamic_index_in_dim(leaf_order, here, 0, keepdims=False)
    own_node = lax.dynamic_index_in_dim(node_order, here, 0, keepdims=False)
    other_node = lax.dynamic_index_in_dim(node_order, across, 0, keepdims=False)
    rotate = jnp.array(list(range(second, first)) + list(range(second)), jnp.int32)
    perm = own_node[rotate]
    partner_perm = other_node[rotate]
    left_pos = own_leaf[perm]
    send_pos = own_leaf[first + partner_perm]
    table = jnp.concatenate([perm, left_pos, send_pos]).astype(jnp.int32)

    recv_leaf = []
    for s in range(first):
        message = select(table, leaves, 2 * first + s)
        recv_leaf.append(from_partner(message, "region", 0))

    level_one, scaled_one, totals_one, sent_one = [], [], [], []
    for s in range(first):
        out, scaled, totals = mix(table, leaves, ("table", first + s), recv_leaf[s][None], ("fixed", 0),
                                  weight_one, ("table", s))
        level_one.append(out)
        scaled_one.append(scaled)
        totals_one.append(totals)
        if s < second:
            sent_one.append(from_partner(out, "region", 1))

    top_log, counts_two = [], []
    adjoint_one = [None] * first
    for j in range(second):
        out, scaled, totals = mix(table, level_one[second + j][None], ("fixed", 0), sent_one[j][None],
                                  ("fixed", 0), weight_two, ("fixed", j))
        top_log.append(out)
        counts, spread = descend(table, top_adjoint, ("fixed", j), scaled, totals, weight_two, ("fixed", j))
        counts_two.append(counts)
        adjoint_one[second + j] = spread
        adjoint_one[j] = from_partner(spread, "region", 1)

    order = list(range(second, first)) + list(range(second))
    counts_one = [None] * first
    returned = [None] * first
    leaf_adjoint = None
    for s in order:
        counts, spread, leaf_adjoint = descend(
            table, adjoint_one[s][None], ("fixed", 0), scaled_one[s], totals_one[s], weight_one,
            ("table", s), buffer_shape=leaves.shape, own_at=first + s, buffer=leaf_adjoint)
        counts_one[s] = counts
        returned[s] = from_partner(spread, "region", 0)
    leaf_adjoint = place(table, leaf_adjoint, [returned[s] for s in order], [2 * first + s for s in order])
    early = batch_sum(jnp.stack(counts_two + [counts_one[s] for s in range(second, first)]), "batch")
    grad_two = early[:second]
    early = (grad_two, early[second:])
    late = batch_sum(jnp.stack([counts_one[s] for s in range(second)]), "batch")
    grad_one = place_grads(table, late, early[1])
    return (jnp.stack(top_log), leaf_adjoint, grad_one, grad_two)


def solution(mesh):
    return jax.shard_map(
        local,
        mesh=mesh,
        in_specs=(
            P("region", "batch", None),
            P(),
            P(),
            P("region", None, None),
            P("region", None, None),
            P("region", "batch", None),
        ),
        out_specs=(
            P("region", "batch", None),
            P("region", "batch", None),
            P("region", None, None),
            P("region", None, None),
        ),
        check_vma=False,
    )
```

```python
import functools

import jax
import jax.numpy as jnp
from jax import lax
from jax.experimental import pallas as pl
from jax.experimental.pallas import tpu as pltpu
from jax.sharding import PartitionSpec as P


HIGHEST = lax.Precision.HIGHEST
VMEM_LIMIT = 48 * 1024 * 1024


def from_partner(value, axis, distance):
    mask = 2**distance
    pairs = [(source, source ^ mask) for source in range(lax.axis_size(axis))]
    return lax.ppermute(value, axis, pairs)


def block(shape, select):
    kind, k = select
    if kind == "table":
        return pl.BlockSpec((None,) + shape, lambda i, t: (t[k], 0, 0))
    return pl.BlockSpec((None,) + shape, lambda i, t: (k, 0, 0))


def rows_block(part, k, select):
    kind, n = select
    if kind == "table":
        return pl.BlockSpec((None, part, k), lambda i, t: (t[n], i, 0))
    return pl.BlockSpec((None, part, k), lambda i, t: (n, i, 0))


PIECES = 4


def whole(shape):
    return pl.BlockSpec(shape, lambda i, t: (0, 0))


ANY = pl.BlockSpec(memory_space=pl.ANY)


def slab_spec(rows, k):
    return pl.BlockSpec((1, rows, k), lambda i, t: (0, 0, 0))


def call(kernel, table, operands, in_specs, out_specs, out_shape, cost, aliases=None, scratch=(), grid=(1,)):
    return pl.pallas_call(
        kernel,
        grid_spec=pltpu.PrefetchScalarGridSpec(
            num_scalar_prefetch=1, grid=grid, in_specs=in_specs, out_specs=out_specs,
            scratch_shapes=list(scratch),
        ),
        out_shape=out_shape,
        input_output_aliases=aliases or {},
        compiler_params=pltpu.CompilerParams(vmem_limit_bytes=VMEM_LIMIT),
        cost_estimate=cost,
    )(table, *operands)


def mix_kernel(table, left, right, weight, out, scaled, totals):
    summed = left[...] + right[...]
    peak = jnp.max(summed, axis=1, keepdims=True)
    p = jnp.exp(summed - peak)
    q = lax.dot_general(p, weight[...], (((1,), (1,)), ((), ())), precision=HIGHEST,
                        preferred_element_type=jnp.float32)
    out[...] = peak + jnp.log(q)
    scaled[...] = p
    totals[...] = q


def mix(table, left, left_sel, right, right_sel, weight, weight_sel):
    rows, k = left.shape[1:]
    part = rows // PIECES
    o = jax.ShapeDtypeStruct((rows, k), jnp.float32)
    cost = pl.CostEstimate(flops=2 * rows * k * k, transcendentals=2 * rows * k,
                           bytes_accessed=4 * (5 * rows * k + k * k))
    return call(mix_kernel, table, (left, right, weight),
                [rows_block(part, k, left_sel), rows_block(part, k, right_sel), block((k, k), weight_sel)],
                [pl.BlockSpec((part, k), lambda i, t: (i, 0))] * 3, [o, o, o], cost, grid=(PIECES,))


def descend_kernel(placing, own_at, table, adjoint, scaled, totals, weight, *rest):
    if placing == 0:
        counts, spread = rest
    elif placing == 1:
        counts, spread, buffer, sems = rest
    else:
        _, counts, spread, buffer, sems = rest
    i = pl.program_id(0)
    ratio = adjoint[...] / totals[...]
    p = scaled[...]
    part = lax.dot_general(ratio, p, (((0,), (0,)), ((), ())), precision=HIGHEST,
                           preferred_element_type=jnp.float32)

    @pl.when(i == 0)
    def _():
        counts[...] = part

    @pl.when(i > 0)
    def _():
        counts[...] += part

    spread[...] = p * jnp.dot(ratio, weight[...], precision=HIGHEST, preferred_element_type=jnp.float32)
    if placing == 0:
        return
    rows = spread.shape[0]
    c = pltpu.make_async_copy(spread, buffer.at[table[own_at], pl.ds(i * rows, rows)], sems.at[0])
    c.start()
    c.wait()


def descend(table, adjoint, adjoint_sel, scaled, totals, weight, weight_sel,
            buffer_shape=None, own_at=None, buffer=None):
    rows, k = scaled.shape
    part = rows // PIECES
    cost = pl.CostEstimate(flops=4 * rows * k * k, transcendentals=0,
                           bytes_accessed=4 * (5 * rows * k + 2 * k * k))
    operands = [adjoint, scaled[None], totals[None], weight]
    in_specs = [rows_block(part, k, adjoint_sel), rows_block(part, k, ("fixed", 0)),
                rows_block(part, k, ("fixed", 0)), block((k, k), weight_sel)]
    out_specs = [whole((k, k)), pl.BlockSpec((part, k), lambda i, t: (i, 0))]
    out_shape = [jax.ShapeDtypeStruct((k, k), jnp.float32), jax.ShapeDtypeStruct((rows, k), jnp.float32)]
    placing, aliases, scratch = 0, None, ()
    if buffer_shape is not None:
        placing = 1 if buffer is None else 2
        out_specs.append(ANY)
        out_shape.append(jax.ShapeDtypeStruct(buffer_shape, jnp.float32))
        scratch = (pltpu.SemaphoreType.DMA((1,)),)
        if buffer is not None:
            operands.append(buffer)
            in_specs.append(ANY)
            aliases = {len(operands): 2}
    kernel = functools.partial(descend_kernel, placing, own_at)
    return call(kernel, table, operands, in_specs, out_specs, out_shape, cost, aliases, scratch,
                grid=(PIECES,))


def place_kernel(positions, table, *rest):
    sources, buffer, sems = rest[:len(positions)], rest[len(positions) + 1], rest[-1]
    copies = [pltpu.make_async_copy(src, buffer.at[pl.ds(table[at], 1)], sems.at[n])
              for n, (src, at) in enumerate(zip(sources, positions))]
    for c in copies:
        c.start()
    for c in copies:
        c.wait()


def place(table, buffer, slabs, positions):
    rows, k = slabs[0].shape
    n = len(slabs)
    cost = pl.CostEstimate(flops=0, transcendentals=0, bytes_accessed=8 * rows * k * n)
    return call(functools.partial(place_kernel, tuple(positions)), table,
                tuple(slab[None] for slab in slabs) + (buffer,),
                [slab_spec(rows, k)] * n + [ANY], ANY,
                jax.ShapeDtypeStruct(buffer.shape, buffer.dtype), cost, aliases={n + 1: 0},
                scratch=(pltpu.SemaphoreType.DMA((n,)),))


def grads_kernel(table, late, early, out, sems):
    pairs = [(late, j, j) for j in range(late.shape[0])]
    pairs += [(early, j, late.shape[0] + j) for j in range(early.shape[0])]
    copies = [pltpu.make_async_copy(src.at[pl.ds(j, 1)], out.at[pl.ds(table[at], 1)], sems.at[n])
              for n, (src, j, at) in enumerate(pairs)]
    for c in copies:
        c.start()
    for c in copies:
        c.wait()


def place_grads(table, late, early):
    n, k, _ = late.shape
    m = early.shape[0]
    cost = pl.CostEstimate(flops=0, transcendentals=0, bytes_accessed=8 * (n + m) * k * k)
    spec = lambda a: pl.BlockSpec(a.shape, lambda i, t: (0, 0, 0))
    return call(grads_kernel, table, (late, early), [spec(late), spec(early)], ANY,
                jax.ShapeDtypeStruct((n + m, k, k), jnp.float32), cost,
                scratch=(pltpu.SemaphoreType.DMA((n + m,)),))


def copy_kernel(table, source, out):
    out[...] = source[...]


def select(table, array, at, pieces=1):
    rows, k = array.shape[1:]
    part = rows // pieces
    cost = pl.CostEstimate(flops=0, transcendentals=0, bytes_accessed=8 * rows * k)
    return call(copy_kernel, table, (array,),
                [pl.BlockSpec((None, part, k), lambda i, t: (t[at], i, 0))],
                pl.BlockSpec((part, k), lambda i, t: (i, 0)),
                jax.ShapeDtypeStruct((rows, k), jnp.float32), cost, grid=(pieces,))


def batch_sum(x, axis):
    if lax.axis_size(axis) != 4:
        return lax.psum(x, axis)
    me = lax.axis_index(axis)
    low = jnp.bitwise_and(me, 1) == 0
    high = jnp.bitwise_and(me, 2) == 0
    flat = x.reshape(-1, x.shape[-1])
    half = flat.shape[0] // 2
    a, b = flat[:half], flat[half:]
    got = from_partner(jnp.where(low, b, a), axis, 0)
    keep = jnp.where(low, a, b) + got
    quarter = half // 2
    c, d = keep[:quarter], keep[quarter:]
    got = from_partner(jnp.where(high, d, c), axis, 1)
    mine = jnp.where(high, c, d) + got
    theirs = from_partner(mine, axis, 1)
    keep = jnp.where(high, jnp.concatenate([mine, theirs]), jnp.concatenate([theirs, mine]))
    theirs = from_partner(keep, axis, 0)
    flat = jnp.where(low, jnp.concatenate([keep, theirs]), jnp.concatenate([theirs, keep]))
    return flat.reshape(x.shape)


def local(leaves, leaf_order, node_order, weight_one, weight_two, top_adjoint):
    here = lax.axis_index("region")
    across = jnp.bitwise_xor(here, jnp.int32(1))
    first = weight_one.shape[0]
    second = weight_two.shape[0]
    own_leaf = lax.dynamic_index_in_dim(leaf_order, here, 0, keepdims=False)
    own_node = lax.dynamic_index_in_dim(node_order, here, 0, keepdims=False)
    other_node = lax.dynamic_index_in_dim(node_order, across, 0, keepdims=False)
    rotate = jnp.array(list(range(second, first)) + list(range(second)), jnp.int32)
    perm = own_node[rotate]
    partner_perm = other_node[rotate]
    left_pos = own_leaf[perm]
    send_pos = own_leaf[first + partner_perm]
    table = jnp.concatenate([perm, left_pos, send_pos]).astype(jnp.int32)

    recv_leaf = []
    for s in range(first):
        message = select(table, leaves, 2 * first + s)
        recv_leaf.append(from_partner(message, "region", 0))

    level_one, scaled_one, totals_one, sent_one = [], [], [], []
    for s in range(first):
        out, scaled, totals = mix(table, leaves, ("table", first + s), recv_leaf[s][None], ("fixed", 0),
                                  weight_one, ("table", s))
        level_one.append(out)
        scaled_one.append(scaled)
        totals_one.append(totals)
        if s < second:
            sent_one.append(from_partner(out, "region", 1))

    top_log, counts_two = [], []
    adjoint_one = [None] * first
    for j in range(second):
        out, scaled, totals = mix(table, level_one[second + j][None], ("fixed", 0), sent_one[j][None],
                                  ("fixed", 0), weight_two, ("fixed", j))
        top_log.append(out)
        counts, spread = descend(table, top_adjoint, ("fixed", j), scaled, totals, weight_two, ("fixed", j))
        counts_two.append(counts)
        adjoint_one[second + j] = spread
        adjoint_one[j] = from_partner(spread, "region", 1)

    order = list(range(second, first)) + list(range(second))
    counts_one = [None] * first
    returned = [None] * first
    leaf_adjoint = None
    for s in order:
        counts, spread, leaf_adjoint = descend(
            table, adjoint_one[s][None], ("fixed", 0), scaled_one[s], totals_one[s], weight_one,
            ("table", s), buffer_shape=leaves.shape, own_at=first + s, buffer=leaf_adjoint)
        counts_one[s] = counts
        returned[s] = from_partner(spread, "region", 0)
    leaf_adjoint = place(table, leaf_adjoint, [returned[s] for s in order], [2 * first + s for s in order])
    early = batch_sum(jnp.stack(counts_two + [counts_one[s] for s in range(second, first)]), "batch")
    grad_two = early[:second]
    early = (grad_two, early[second:])
    late = batch_sum(jnp.stack([counts_one[s] for s in range(second)]), "batch")
    grad_one = place_grads(table, late, early[1])
    return (jnp.stack(top_log), leaf_adjoint, grad_one, grad_two)


def solution(mesh):
    return jax.shard_map(
        local,
        mesh=mesh,
        in_specs=(
            P("region", "batch", None),
            P(),
            P(),
            P("region", None, None),
            P("region", None, None),
            P("region", "batch", None),
        ),
        out_specs=(
            P("region", "batch", None),
            P("region", "batch", None),
            P("region", None, None),
            P("region", None, None),
        ),
        check_vma=False,
    )
```

```python
import functools

import jax
import jax.numpy as jnp
from jax import lax
from jax.experimental import pallas as pl
from jax.experimental.pallas import tpu as pltpu
from jax.sharding import PartitionSpec as P


HIGHEST = lax.Precision.HIGHEST
VMEM_LIMIT = 48 * 1024 * 1024


def from_partner(value, axis, distance):
    mask = 2**distance
    pairs = [(source, source ^ mask) for source in range(lax.axis_size(axis))]
    return lax.ppermute(value, axis, pairs)


def block(shape, select):
    kind, k = select
    if kind == "table":
        return pl.BlockSpec((None,) + shape, lambda i, t: (t[k], 0, 0))
    return pl.BlockSpec((None,) + shape, lambda i, t: (k, 0, 0))


def whole(shape):
    return pl.BlockSpec(shape, lambda i, t: (0, 0))


ANY = pl.BlockSpec(memory_space=pl.ANY)


def slab_spec(rows, k):
    return pl.BlockSpec((1, rows, k), lambda i, t: (0, 0, 0))


def call(kernel, table, operands, in_specs, out_specs, out_shape, cost, aliases=None, scratch=(), grid=(1,)):
    return pl.pallas_call(
        kernel,
        grid_spec=pltpu.PrefetchScalarGridSpec(
            num_scalar_prefetch=1, grid=grid, in_specs=in_specs, out_specs=out_specs,
            scratch_shapes=list(scratch),
        ),
        out_shape=out_shape,
        input_output_aliases=aliases or {},
        compiler_params=pltpu.CompilerParams(vmem_limit_bytes=VMEM_LIMIT),
        cost_estimate=cost,
    )(table, *operands)


def mix_kernel(table, left, right, weight, out, scaled, totals):
    summed = left[...] + right[...]
    peak = jnp.max(summed, axis=1, keepdims=True)
    p = jnp.exp(summed - peak)
    q = lax.dot_general(p, weight[...], (((1,), (1,)), ((), ())), precision=HIGHEST,
                        preferred_element_type=jnp.float32)
    out[...] = peak + jnp.log(q)
    scaled[...] = p
    totals[...] = q


def mix(table, left, left_sel, right, right_sel, weight, weight_sel):
    rows, k = left.shape[1:]
    o = jax.ShapeDtypeStruct((rows, k), jnp.float32)
    cost = pl.CostEstimate(flops=2 * rows * k * k, transcendentals=2 * rows * k,
                           bytes_accessed=4 * (5 * rows * k + k * k))
    return call(mix_kernel, table, (left, right, weight),
                [block((rows, k), left_sel), block((rows, k), right_sel), block((k, k), weight_sel)],
                [whole((rows, k))] * 3, [o, o, o], cost)


def descend_kernel(placing, own_at, table, adjoint, scaled, totals, weight, *rest):
    if placing == 0:
        counts, spread = rest
    elif placing == 1:
        counts, spread, buffer, sems = rest
    else:
        _, counts, spread, buffer, sems = rest
    ratio = adjoint[...] / totals[...]
    p = scaled[...]
    counts[...] = lax.dot_general(ratio, p, (((0,), (0,)), ((), ())), precision=HIGHEST,
                                  preferred_element_type=jnp.float32)
    spread[...] = p * jnp.dot(ratio, weight[...], precision=HIGHEST, preferred_element_type=jnp.float32)
    if placing == 0:
        return
    c = pltpu.make_async_copy(spread, buffer.at[table[own_at]], sems.at[0])
    c.start()
    c.wait()


def descend(table, adjoint, adjoint_sel, scaled, totals, weight, weight_sel,
            buffer_shape=None, own_at=None, buffer=None):
    rows, k = scaled.shape
    cost = pl.CostEstimate(flops=4 * rows * k * k, transcendentals=0,
                           bytes_accessed=4 * (5 * rows * k + 2 * k * k))
    operands = [adjoint, scaled[None], totals[None], weight]
    in_specs = [block((rows, k), adjoint_sel), block((rows, k), ("fixed", 0)),
                block((rows, k), ("fixed", 0)), block((k, k), weight_sel)]
    out_specs = [whole((k, k)), whole((rows, k))]
    out_shape = [jax.ShapeDtypeStruct((k, k), jnp.float32), jax.ShapeDtypeStruct((rows, k), jnp.float32)]
    placing, aliases, scratch = 0, None, ()
    if buffer_shape is not None:
        placing = 1 if buffer is None else 2
        out_specs.append(ANY)
        out_shape.append(jax.ShapeDtypeStruct(buffer_shape, jnp.float32))
        scratch = (pltpu.SemaphoreType.DMA((1,)),)
        if buffer is not None:
            operands.append(buffer)
            in_specs.append(ANY)
            aliases = {len(operands): 2}
    kernel = functools.partial(descend_kernel, placing, own_at)
    return call(kernel, table, operands, in_specs, out_specs, out_shape, cost, aliases, scratch)


def place_kernel(positions, table, *rest):
    sources, buffer, sems = rest[:len(positions)], rest[len(positions) + 1], rest[-1]
    copies = [pltpu.make_async_copy(src, buffer.at[pl.ds(table[at], 1)], sems.at[n])
              for n, (src, at) in enumerate(zip(sources, positions))]
    for c in copies:
        c.start()
    for c in copies:
        c.wait()


def place(table, buffer, slabs, positions):
    rows, k = slabs[0].shape
    n = len(slabs)
    cost = pl.CostEstimate(flops=0, transcendentals=0, bytes_accessed=8 * rows * k * n)
    return call(functools.partial(place_kernel, tuple(positions)), table,
                tuple(slab[None] for slab in slabs) + (buffer,),
                [slab_spec(rows, k)] * n + [ANY], ANY,
                jax.ShapeDtypeStruct(buffer.shape, buffer.dtype), cost, aliases={n + 1: 0},
                scratch=(pltpu.SemaphoreType.DMA((n,)),))


def grads_kernel(table, late, early, out, sems):
    pairs = [(late, j, j) for j in range(late.shape[0])]
    pairs += [(early, j, late.shape[0] + j) for j in range(early.shape[0])]
    copies = [pltpu.make_async_copy(src.at[pl.ds(j, 1)], out.at[pl.ds(table[at], 1)], sems.at[n])
              for n, (src, j, at) in enumerate(pairs)]
    for c in copies:
        c.start()
    for c in copies:
        c.wait()


def place_grads(table, late, early):
    n, k, _ = late.shape
    m = early.shape[0]
    cost = pl.CostEstimate(flops=0, transcendentals=0, bytes_accessed=8 * (n + m) * k * k)
    spec = lambda a: pl.BlockSpec(a.shape, lambda i, t: (0, 0, 0))
    return call(grads_kernel, table, (late, early), [spec(late), spec(early)], ANY,
                jax.ShapeDtypeStruct((n + m, k, k), jnp.float32), cost,
                scratch=(pltpu.SemaphoreType.DMA((n + m,)),))


def copy_kernel(table, source, out):
    out[...] = source[...]


def select(table, array, at, pieces=1):
    rows, k = array.shape[1:]
    part = rows // pieces
    cost = pl.CostEstimate(flops=0, transcendentals=0, bytes_accessed=8 * rows * k)
    return call(copy_kernel, table, (array,),
                [pl.BlockSpec((None, part, k), lambda i, t: (t[at], i, 0))],
                pl.BlockSpec((part, k), lambda i, t: (i, 0)),
                jax.ShapeDtypeStruct((rows, k), jnp.float32), cost, grid=(pieces,))


def batch_sum(x, axis):
    if lax.axis_size(axis) != 4:
        return lax.psum(x, axis)
    me = lax.axis_index(axis)
    low = jnp.bitwise_and(me, 1) == 0
    high = jnp.bitwise_and(me, 2) == 0
    flat = x.reshape(-1, x.shape[-1])
    half = flat.shape[0] // 2
    a, b = flat[:half], flat[half:]
    got = from_partner(jnp.where(low, b, a), axis, 0)
    keep = jnp.where(low, a, b) + got
    quarter = half // 2
    c, d = keep[:quarter], keep[quarter:]
    got = from_partner(jnp.where(high, d, c), axis, 1)
    mine = jnp.where(high, c, d) + got
    theirs = from_partner(mine, axis, 1)
    keep = jnp.where(high, jnp.concatenate([mine, theirs]), jnp.concatenate([theirs, mine]))
    theirs = from_partner(keep, axis, 0)
    flat = jnp.where(low, jnp.concatenate([keep, theirs]), jnp.concatenate([theirs, keep]))
    return flat.reshape(x.shape)


def local(leaves, leaf_order, node_order, weight_one, weight_two, top_adjoint):
    here = lax.axis_index("region")
    across = jnp.bitwise_xor(here, jnp.int32(1))
    first = weight_one.shape[0]
    second = weight_two.shape[0]
    regions = jnp.arange(leaf_order.shape[0], dtype=jnp.int32)[:, None]
    own_leaf = jnp.sum(jnp.where(regions == here, leaf_order, 0), axis=0)
    own_node = jnp.sum(jnp.where(regions == here, node_order, 0), axis=0)
    other_node = jnp.sum(jnp.where(regions == across, node_order, 0), axis=0)
    perm = jnp.concatenate([own_node[second:], own_node[:second]])
    partner_perm = jnp.concatenate([other_node[second:], other_node[:second]])
    leaf_slots = jnp.arange(leaf_order.shape[1], dtype=jnp.int32)[None, :]
    left_pos = jnp.sum(jnp.where(leaf_slots == perm[:, None], own_leaf[None, :], 0), axis=1)
    send_pos = jnp.sum(jnp.where(leaf_slots == first + partner_perm[:, None], own_leaf[None, :], 0), axis=1)
    table = jnp.concatenate([perm, left_pos, send_pos]).astype(jnp.int32)

    recv_leaf = []
    for s in range(first):
        message = select(table, leaves, 2 * first + s)
        recv_leaf.append(from_partner(message, "region", 0))

    level_one, scaled_one, totals_one, sent_one = [], [], [], []
    for s in range(first):
        out, scaled, totals = mix(table, leaves, ("table", first + s), recv_leaf[s][None], ("fixed", 0),
                                  weight_one, ("table", s))
        level_one.append(out)
        scaled_one.append(scaled)
        totals_one.append(totals)
        if s < second:
            sent_one.append(from_partner(out, "region", 1))

    top_log, counts_two = [], []
    adjoint_one = [None] * first
    for j in range(second):
        out, scaled, totals = mix(table, level_one[second + j][None], ("fixed", 0), sent_one[j][None],
                                  ("fixed", 0), weight_two, ("fixed", j))
        top_log.append(out)
        counts, spread = descend(table, top_adjoint, ("fixed", j), scaled, totals, weight_two, ("fixed", j))
        counts_two.append(counts)
        adjoint_one[second + j] = spread
        adjoint_one[j] = from_partner(spread, "region", 1)

    order = list(range(second, first)) + list(range(second))
    counts_one = [None] * first
    returned = [None] * first
    leaf_adjoint = None
    for s in order:
        counts, spread, leaf_adjoint = descend(
            table, adjoint_one[s][None], ("fixed", 0), scaled_one[s], totals_one[s], weight_one,
            ("table", s), buffer_shape=leaves.shape, own_at=first + s, buffer=leaf_adjoint)
        counts_one[s] = counts
        returned[s] = from_partner(spread, "region", 0)
    leaf_adjoint = place(table, leaf_adjoint, [returned[s] for s in order], [2 * first + s for s in order])
    early = batch_sum(jnp.stack(counts_two + [counts_one[s] for s in range(second, first)]), "batch")
    grad_two = early[:second]
    early = (grad_two, early[second:])
    late = batch_sum(jnp.stack([counts_one[s] for s in range(second)]), "batch")
    grad_one = place_grads(table, late, early[1])
    return (jnp.stack(top_log), leaf_adjoint, grad_one, grad_two)


def solution(mesh):
    return jax.shard_map(
        local,
        mesh=mesh,
        in_specs=(
            P("region", "batch", None),
            P(),
            P(),
            P("region", None, None),
            P("region", None, None),
            P("region", "batch", None),
        ),
        out_specs=(
            P("region", "batch", None),
            P("region", "batch", None),
            P("region", None, None),
            P("region", None, None),
        ),
        check_vma=False,
    )
```

```python
import functools

import jax
import jax.numpy as jnp
from jax import lax
from jax.experimental import pallas as pl
from jax.experimental.pallas import tpu as pltpu
from jax.sharding import PartitionSpec as P


HIGHEST = lax.Precision.HIGHEST
VMEM_LIMIT = 48 * 1024 * 1024


def from_partner(value, axis, distance):
    mask = 2**distance
    pairs = [(source, source ^ mask) for source in range(lax.axis_size(axis))]
    return lax.ppermute(value, axis, pairs)


def block(shape, select):
    kind, k = select
    if kind == "table":
        return pl.BlockSpec((None,) + shape, lambda i, t: (t[k], 0, 0))
    return pl.BlockSpec((None,) + shape, lambda i, t: (k, 0, 0))


def whole(shape):
    return pl.BlockSpec(shape, lambda i, t: (0, 0))


ANY = pl.BlockSpec(memory_space=pl.ANY)


def slab_spec(rows, k):
    return pl.BlockSpec((1, rows, k), lambda i, t: (0, 0, 0))


def call(kernel, table, operands, in_specs, out_specs, out_shape, cost, aliases=None, scratch=(), grid=(1,)):
    return pl.pallas_call(
        kernel,
        grid_spec=pltpu.PrefetchScalarGridSpec(
            num_scalar_prefetch=1, grid=grid, in_specs=in_specs, out_specs=out_specs,
            scratch_shapes=list(scratch),
        ),
        out_shape=out_shape,
        input_output_aliases=aliases or {},
        compiler_params=pltpu.CompilerParams(vmem_limit_bytes=VMEM_LIMIT),
        cost_estimate=cost,
    )(table, *operands)


def mix_kernel(table, left, right, weight, out, scaled, totals):
    summed = left[...] + right[...]
    peak = jnp.max(summed, axis=1, keepdims=True)
    p = jnp.exp(summed - peak)
    q = lax.dot_general(p, weight[...], (((1,), (1,)), ((), ())), precision=HIGHEST,
                        preferred_element_type=jnp.float32)
    out[...] = peak + jnp.log(q)
    scaled[...] = p
    totals[...] = q


def mix(table, left, left_sel, right, right_sel, weight, weight_sel):
    rows, k = left.shape[1:]
    o = jax.ShapeDtypeStruct((rows, k), jnp.float32)
    cost = pl.CostEstimate(flops=2 * rows * k * k, transcendentals=2 * rows * k,
                           bytes_accessed=4 * (5 * rows * k + k * k))
    return call(mix_kernel, table, (left, right, weight),
                [block((rows, k), left_sel), block((rows, k), right_sel), block((k, k), weight_sel)],
                [whole((rows, k))] * 3, [o, o, o], cost)


def descend_kernel(placing, own_at, table, adjoint, scaled, totals, weight, *rest):
    if placing == 0:
        counts, spread = rest
    elif placing == 1:
        counts, spread, buffer, sems = rest
    else:
        _, counts, spread, buffer, sems = rest
    ratio = adjoint[...] / totals[...]
    p = scaled[...]
    counts[...] = lax.dot_general(ratio, p, (((0,), (0,)), ((), ())), precision=HIGHEST,
                                  preferred_element_type=jnp.float32)
    spread[...] = p * jnp.dot(ratio, weight[...], precision=HIGHEST, preferred_element_type=jnp.float32)
    if placing == 0:
        return
    c = pltpu.make_async_copy(spread, buffer.at[table[own_at]], sems.at[0])
    c.start()
    c.wait()


def descend(table, adjoint, adjoint_sel, scaled, totals, weight, weight_sel,
            buffer_shape=None, own_at=None, buffer=None):
    rows, k = scaled.shape
    cost = pl.CostEstimate(flops=4 * rows * k * k, transcendentals=0,
                           bytes_accessed=4 * (5 * rows * k + 2 * k * k))
    operands = [adjoint, scaled[None], totals[None], weight]
    in_specs = [block((rows, k), adjoint_sel), block((rows, k), ("fixed", 0)),
                block((rows, k), ("fixed", 0)), block((k, k), weight_sel)]
    out_specs = [whole((k, k)), whole((rows, k))]
    out_shape = [jax.ShapeDtypeStruct((k, k), jnp.float32), jax.ShapeDtypeStruct((rows, k), jnp.float32)]
    placing, aliases, scratch = 0, None, ()
    if buffer_shape is not None:
        placing = 1 if buffer is None else 2
        out_specs.append(ANY)
        out_shape.append(jax.ShapeDtypeStruct(buffer_shape, jnp.float32))
        scratch = (pltpu.SemaphoreType.DMA((1,)),)
        if buffer is not None:
            operands.append(buffer)
            in_specs.append(ANY)
            aliases = {len(operands): 2}
    kernel = functools.partial(descend_kernel, placing, own_at)
    return call(kernel, table, operands, in_specs, out_specs, out_shape, cost, aliases, scratch)


def place_kernel(positions, table, *rest):
    sources, buffer, sems = rest[:len(positions)], rest[len(positions) + 1], rest[-1]
    copies = [pltpu.make_async_copy(src, buffer.at[pl.ds(table[at], 1)], sems.at[n])
              for n, (src, at) in enumerate(zip(sources, positions))]
    for c in copies:
        c.start()
    for c in copies:
        c.wait()


def place(table, buffer, slabs, positions):
    rows, k = slabs[0].shape
    n = len(slabs)
    cost = pl.CostEstimate(flops=0, transcendentals=0, bytes_accessed=8 * rows * k * n)
    return call(functools.partial(place_kernel, tuple(positions)), table,
                tuple(slab[None] for slab in slabs) + (buffer,),
                [slab_spec(rows, k)] * n + [ANY], ANY,
                jax.ShapeDtypeStruct(buffer.shape, buffer.dtype), cost, aliases={n + 1: 0},
                scratch=(pltpu.SemaphoreType.DMA((n,)),))


def grads_kernel(table, late, early, out, sems):
    pairs = [(late, j, j) for j in range(late.shape[0])]
    pairs += [(early, j, late.shape[0] + j) for j in range(early.shape[0])]
    copies = [pltpu.make_async_copy(src.at[pl.ds(j, 1)], out.at[pl.ds(table[at], 1)], sems.at[n])
              for n, (src, j, at) in enumerate(pairs)]
    for c in copies:
        c.start()
    for c in copies:
        c.wait()


def place_grads(table, late, early):
    n, k, _ = late.shape
    m = early.shape[0]
    cost = pl.CostEstimate(flops=0, transcendentals=0, bytes_accessed=8 * (n + m) * k * k)
    spec = lambda a: pl.BlockSpec(a.shape, lambda i, t: (0, 0, 0))
    return call(grads_kernel, table, (late, early), [spec(late), spec(early)], ANY,
                jax.ShapeDtypeStruct((n + m, k, k), jnp.float32), cost,
                scratch=(pltpu.SemaphoreType.DMA((n + m,)),))


def copy_kernel(table, source, out):
    out[...] = source[...]


def select(table, array, at, pieces=1):
    rows, k = array.shape[1:]
    part = rows // pieces
    cost = pl.CostEstimate(flops=0, transcendentals=0, bytes_accessed=8 * rows * k)
    return call(copy_kernel, table, (array,),
                [pl.BlockSpec((None, part, k), lambda i, t: (t[at], i, 0))],
                pl.BlockSpec((part, k), lambda i, t: (i, 0)),
                jax.ShapeDtypeStruct((rows, k), jnp.float32), cost, grid=(pieces,))


def batch_sum(x, axis):
    if lax.axis_size(axis) != 4:
        return lax.psum(x, axis)
    me = lax.axis_index(axis)
    low = jnp.bitwise_and(me, 1) == 0
    high = jnp.bitwise_and(me, 2) == 0
    flat = x.reshape(-1, x.shape[-1])
    half = flat.shape[0] // 2
    a, b = flat[:half], flat[half:]
    got = from_partner(jnp.where(low, b, a), axis, 0)
    keep = jnp.where(low, a, b) + got
    quarter = half // 2
    c, d = keep[:quarter], keep[quarter:]
    got = from_partner(jnp.where(high, d, c), axis, 1)
    mine = jnp.where(high, c, d) + got
    theirs = from_partner(mine, axis, 1)
    keep = jnp.where(high, jnp.concatenate([mine, theirs]), jnp.concatenate([theirs, mine]))
    theirs = from_partner(keep, axis, 0)
    flat = jnp.where(low, jnp.concatenate([keep, theirs]), jnp.concatenate([theirs, keep]))
    return flat.reshape(x.shape)


def shift_from(value, axis, shift):
    n = lax.axis_size(axis)
    return lax.ppermute(value, axis, [(source, (source + shift) % n) for source in range(n)])


def batch_sum_wide(x, axis):
    n = lax.axis_size(axis)
    me = lax.axis_index(axis)
    flat = x.reshape(n, -1, x.shape[-1])
    shifts = range(1, n)
    got = [shift_from(lax.dynamic_index_in_dim(flat, (me + k) % n, 0, keepdims=False), axis, k) for k in shifts]
    total = lax.dynamic_index_in_dim(flat, me, 0, keepdims=False)
    for g in got:
        total = total + g
    back = [shift_from(total, axis, k) for k in shifts]
    pieces = [total] + back
    rows = []
    for j in range(n):
        owner = (me - j) % n
        piece = pieces[0]
        for k in shifts:
            piece = jnp.where(owner == k, pieces[k], piece)
        rows.append(piece)
    return jnp.stack(rows).reshape(x.shape)


def local(leaves, leaf_order, node_order, weight_one, weight_two, top_adjoint):
    here = lax.axis_index("region")
    across = jnp.bitwise_xor(here, jnp.int32(1))
    first = weight_one.shape[0]
    second = weight_two.shape[0]
    regions = jnp.arange(leaf_order.shape[0], dtype=jnp.int32)[:, None]
    own_leaf = jnp.sum(jnp.where(regions == here, leaf_order, 0), axis=0)
    own_node = jnp.sum(jnp.where(regions == here, node_order, 0), axis=0)
    other_node = jnp.sum(jnp.where(regions == across, node_order, 0), axis=0)
    perm = jnp.concatenate([own_node[second:], own_node[:second]])
    partner_perm = jnp.concatenate([other_node[second:], other_node[:second]])
    leaf_slots = jnp.arange(leaf_order.shape[1], dtype=jnp.int32)[None, :]
    left_pos = jnp.sum(jnp.where(leaf_slots == perm[:, None], own_leaf[None, :], 0), axis=1)
    send_pos = jnp.sum(jnp.where(leaf_slots == first + partner_perm[:, None], own_leaf[None, :], 0), axis=1)
    table = jnp.concatenate([perm, left_pos, send_pos]).astype(jnp.int32)

    recv_leaf = []
    for s in range(first):
        message = select(table, leaves, 2 * first + s)
        recv_leaf.append(from_partner(message, "region", 0))

    level_one, scaled_one, totals_one, sent_one = [], [], [], []
    for s in range(first):
        out, scaled, totals = mix(table, leaves, ("table", first + s), recv_leaf[s][None], ("fixed", 0),
                                  weight_one, ("table", s))
        level_one.append(out)
        scaled_one.append(scaled)
        totals_one.append(totals)
        if s < second:
            sent_one.append(from_partner(out, "region", 1))

    top_log, counts_two = [], []
    adjoint_one = [None] * first
    for j in range(second):
        out, scaled, totals = mix(table, level_one[second + j][None], ("fixed", 0), sent_one[j][None],
                                  ("fixed", 0), weight_two, ("fixed", j))
        top_log.append(out)
        counts, spread = descend(table, top_adjoint, ("fixed", j), scaled, totals, weight_two, ("fixed", j))
        counts_two.append(counts)
        adjoint_one[second + j] = spread
        adjoint_one[j] = from_partner(spread, "region", 1)

    order = list(range(second, first)) + list(range(second))
    counts_one = [None] * first
    returned = [None] * first
    leaf_adjoint = None
    for s in order:
        counts, spread, leaf_adjoint = descend(
            table, adjoint_one[s][None], ("fixed", 0), scaled_one[s], totals_one[s], weight_one,
            ("table", s), buffer_shape=leaves.shape, own_at=first + s, buffer=leaf_adjoint)
        counts_one[s] = counts
        returned[s] = from_partner(spread, "region", 0)
    leaf_adjoint = place(table, leaf_adjoint, [returned[s] for s in order], [2 * first + s for s in order])
    early = batch_sum(jnp.stack(counts_two + [counts_one[s] for s in range(second, first)]), "batch")
    grad_two = early[:second]
    early = (grad_two, early[second:])
    late = batch_sum_wide(jnp.stack([counts_one[s] for s in range(second)]), "batch")
    grad_one = place_grads(table, late, early[1])
    return (jnp.stack(top_log), leaf_adjoint, grad_one, grad_two)


def solution(mesh):
    return jax.shard_map(
        local,
        mesh=mesh,
        in_specs=(
            P("region", "batch", None),
            P(),
            P(),
            P("region", None, None),
            P("region", None, None),
            P("region", "batch", None),
        ),
        out_specs=(
            P("region", "batch", None),
            P("region", "batch", None),
            P("region", None, None),
            P("region", None, None),
        ),
        check_vma=False,
    )
```
